512 devices in a mesh: path: 64 (over x, z_hi, y, core), trade: 8 (over z_lo).
Axes of the slice: x: 4, y: 4, z: 16 (z_hi: 2, z_lo: 8; z = z_hi * 8 + z_lo), core: 2. Of those that a mesh axis runs over, the one named last changes fastest.
Arguments:
- drivers: bfloat16 [8192, 4096], P('path'), may hold values from -5 to 5
- loadings: bfloat16 [4096, 8192], P('path', 'trade'), may hold values from -0.09375 to 0.09375
- start_state: bfloat16 [8192, 8192], P('path', 'trade'), may hold values from -4 to 4
- coeffs: bfloat16 [8192, 64], P('trade'), may hold values from -1 to 1
- trade_col: int32 [8192], P('trade'), may hold values from 0 to 8191, as said below
- trade_ns: int32 [8192], P('trade'), may hold values from 0 to 2047, as said below
- ns_cp: int32 [2048], P('trade'), may hold values from 0 to 255
Outputs:
- cp_exposure: float32 [256, 8192], P('trade', 'path')
The draws below stay inside these ranges and needn't reach their ends.
Inputs may be any that keep to these rules, and one draw needn't show every extreme that they name: `trade_ns`: each netting set holds 1 to 32 trades, at least one exactly 32. `trade_col`: the trades of one index of trade have exactly 128 trades reading from each of the aligned blocks of 1024 factors held by one index of trade.
All inputs are finite; a program needn't handle non-finite values.
Results may differ from the reference program's by a relative error of at most 0.0059.
The reference program's roundings to bfloat16 on the way count: a program that leaves them out, or rounds other values in their place, can miss the bound.
Values may be sent and summed in bfloat16 or wider, within the bound.
No kernel may reach another device: no remote copies, remote signals or barrier semaphores. Data moves between devices by JAX's collectives and lax.ppermute only.
A program may use at most 64 MiB of HBM per device.

```python
import jax
import jax.numpy as jnp
from jax import lax

PATH_DEV = 128
DRIVERS = 4096
FACTORS = 8192
NBASIS = 64
TRADE_DEV = 1024
MOST = 32
PATHS = 8192
TRADES = 8192
NS = 2048
CP = 256
N_TRADE = 8


def draw_trade_col(key, part):
    width = FACTORS // N_TRADE
    keys = jax.random.split(jax.random.fold_in(key, 11), N_TRADE)
    orders = jax.vmap(lambda one_key: jax.random.permutation(one_key, TRADE_DEV))(keys)
    holder = orders * N_TRADE // TRADE_DEV
    offsets = jax.random.randint(jax.random.fold_in(key, 12), (N_TRADE, TRADE_DEV), 0, width)
    offsets = jnp.where(orders == 0, 0, offsets)
    offsets = jnp.where(orders == TRADE_DEV - 1, width - 1, offsets)
    return (holder * width + offsets).astype(jnp.int32).reshape(TRADES)


def draw_trade_ns(key, part):
    sets_each = MOST // 2
    groups = TRADES // (2 * MOST)
    inner = jnp.arange(1, sets_each, dtype=jnp.int32)
    jitter = jax.random.randint(jax.random.fold_in(key, 21), (groups, sets_each - 1), -1, 2).astype(jnp.int32)
    bounds = 4 * inner[None, :] + jitter
    first = jnp.where(inner == 1, MOST, MOST + 2 * (inner - 1)).astype(jnp.int32)
    group_ids = jnp.arange(groups, dtype=jnp.int32)
    bounds = jnp.where(group_ids[:, None] == 0, first[None, :], bounds)
    places = jnp.arange(TRADES, dtype=jnp.int32)
    group = places // (2 * MOST)
    rest = places % (2 * MOST)
    local = jnp.sum((rest[:, None] >= bounds[group]).astype(jnp.int32), axis=1)
    ids = group * sets_each + local
    return ids.reshape(TRADE_DEV, N_TRADE).T.reshape(TRADES).astype(jnp.int32)


def touch_ends(values, own_key, least, high):
    index_at = [jax.random.randint(jax.random.fold_in(own_key, axis), (), 0, length) for axis, length in enumerate(values.shape)]
    longest = values.shape.index(max(values.shape))
    next_to = index_at[:longest] + [(index_at[longest] + 1) % values.shape[longest]] + index_at[longest + 1:]
    return values.at[tuple(index_at)].set(least).at[tuple(next_to)].set(high)


def levels(own_key, shape, pieces, low, high):
    loudness, own = 1.0, jax.random.fold_in(own_key, 6)
    for dim, blocks in pieces:
        heights = jnp.exp(jax.random.uniform(jax.random.fold_in(own, dim), (blocks,), jnp.float32, low / len(pieces), high / len(pieces)))
        loudness = loudness * jnp.repeat(heights, shape[dim] // blocks).reshape([-1 if axis == dim else 1 for axis in range(len(shape))])
    return loudness


def normal_values(rng, shape, scale, limit, cuts=(), kind=jnp.bfloat16):
    level = levels(rng, shape, cuts, -0.22, 0.18) if cuts else 1.0
    drawn = jax.random.normal(rng, shape, jnp.float32) * scale * level
    return jnp.minimum(jnp.maximum(drawn, -limit), limit).astype(kind)


def setup_inputs(seed: int = 0) -> dict:
    key_list = jax.random.split(jax.random.key(seed), 8)
    drivers = normal_values(key_list[0], (PATHS, DRIVERS), 1.0, 5.0, ((0, 64),))
    loadings = normal_values(key_list[1], (DRIVERS, FACTORS), DRIVERS ** -0.5, 0.09375, ((0, 64), (1, 8)))
    start_state = normal_values(key_list[2], (PATHS, FACTORS), 1.0, 4.0, ((0, 64), (1, 8)))
    coeffs = normal_values(key_list[3], (TRADES, NBASIS), 0.15, 1.0, ((0, 8),))
    trade_col = draw_trade_col(jax.random.fold_in(key_list[7], 71), 0)
    trade_ns = draw_trade_ns(jax.random.fold_in(key_list[7], 71), 0)
    ns_cp = touch_ends(jax.random.randint(key_list[6], (NS,), 0, CP), jax.random.fold_in(key_list[6], 1), 0, CP - 1).astype(jnp.int32)
    return dict(drivers=drivers, loadings=loadings, start_state=start_state, coeffs=coeffs, trade_col=trade_col, trade_ns=trade_ns, ns_cp=ns_cp)


def valuation(chosen, coeffs):
    count = chosen.shape[1]
    rows = chosen.shape[0]
    block = min(128, count)
    blocks = count // block
    orders = jnp.arange(NBASIS, dtype=jnp.float32)

    def one_block(pair):
        factor_part, coeff_part = pair
        theta = jnp.arccos(jnp.tanh(factor_part.astype(jnp.float32) * 0.5))
        basis = jnp.cos(theta[:, :, None] * orders[None, None, :])
        return jnp.einsum("ptk,tk->pt", basis, coeff_part.astype(jnp.float32), precision=lax.Precision.HIGHEST)

    factor_blocks = chosen.reshape(rows, blocks, block).transpose(1, 0, 2)
    coeff_blocks = coeffs.reshape(blocks, block, NBASIS)
    values = lax.map(one_block, (factor_blocks, coeff_blocks))
    return values.transpose(1, 0, 2).reshape(rows, count).astype(jnp.bfloat16)


def reference(drivers, loadings, start_state, coeffs, trade_col, trade_ns, ns_cp):
    net_table = (trade_ns[:, None] == jnp.arange(NS, dtype=jnp.int32)[None, :]).astype(jnp.float32)
    cp_table = (ns_cp[:, None] == jnp.arange(CP, dtype=jnp.int32)[None, :]).astype(jnp.float32)
    loads_wide = loadings.astype(jnp.float32)
    blocks = PATHS // PATH_DEV

    def one_slab(index):
        begin = (index * PATH_DEV).astype(jnp.int32)
        shocks = lax.dynamic_slice_in_dim(drivers, begin, PATH_DEV, 0).astype(jnp.float32)
        before = lax.dynamic_slice_in_dim(start_state, begin, PATH_DEV, 0)
        moved = jnp.dot(shocks, loads_wide, precision=lax.Precision.HIGHEST)
        factors = (before.astype(jnp.float32) + moved).astype(jnp.bfloat16)
        chosen = jnp.take(factors, trade_col, axis=1)
        values = valuation(chosen, coeffs)
        netting = jnp.dot(values.astype(jnp.float32), net_table, precision=lax.Precision.HIGHEST)
        positive = jnp.maximum(netting, 0.0).astype(jnp.bfloat16)
        return jnp.dot(positive.astype(jnp.float32), cp_table, precision=lax.Precision.HIGHEST).T

    slabs = lax.map(one_slab, jnp.arange(blocks, dtype=jnp.int32))
    return slabs.transpose(1, 0, 2).reshape(CP, PATHS)
```

```python
import jax
import jax.numpy as jnp
from jax import lax
from jax.sharding import PartitionSpec as P

CP_DEV = 32


def clenshaw(chosen, coeffs_t):
    x = jnp.tanh(chosen.astype(jnp.float32) * 0.5)
    twice = x + x
    terms = coeffs_t.shape[0]
    b1 = jnp.zeros_like(x)
    b2 = jnp.zeros_like(x)
    for k in range(terms - 1, 0, -1):
        b1, b2 = coeffs_t[k][None, :] + twice * b1 - b2, b1
    return (coeffs_t[0][None, :] + x * b1 - b2).astype(jnp.bfloat16)


def regroup(trade_col, width, owners):
    count = trade_col.shape[0]
    per = count // owners
    block = trade_col // width
    onehot = (block[:, None] == jnp.arange(owners, dtype=jnp.int32)[None, :]).astype(jnp.bfloat16)
    lower = (
        jnp.arange(count, dtype=jnp.int32)[:, None] >= jnp.arange(count, dtype=jnp.int32)[None, :]
    ).astype(jnp.bfloat16)
    running = jnp.dot(lower, onehot, preferred_element_type=jnp.float32)
    rank = jnp.sum(running * onehot.astype(jnp.float32), axis=1).astype(jnp.int32) - 1
    slot = block * per + rank
    return (slot[:, None] == jnp.arange(count, dtype=jnp.int32)[None, :]).astype(jnp.float32)


def per_device(drivers, loadings, start_state, coeffs, trade_col, trade_ns, ns_cp):
    owners = lax.axis_size("trade")
    width = start_state.shape[1]
    count, terms = coeffs.shape
    per = count // owners

    place = regroup(trade_col, width, owners)
    offset = (trade_col % width).astype(jnp.float32)
    table = jnp.concatenate(
        [coeffs.astype(jnp.float32), offset[:, None], trade_ns.astype(jnp.float32)[:, None]], axis=1
    )
    sent = jnp.dot(place.T, table, precision=lax.Precision.HIGHEST)
    got = lax.all_to_all(sent.reshape(owners, per, terms + 2), "trade", 0, 0, tiled=False)
    got = got.reshape(count, terms + 2)
    got_coeffs = got[:, :terms].astype(jnp.bfloat16)
    got_col = got[:, terms].astype(jnp.int32)
    got_ns = got[:, terms + 1].astype(jnp.int32)

    moved = jnp.dot(
        drivers,
        lax.all_gather(loadings, "path", axis=0, tiled=True),
        preferred_element_type=jnp.float32,
    )
    factors = (start_state.astype(jnp.float32) + moved).astype(jnp.bfloat16)
    pick = (jnp.arange(width, dtype=jnp.int32)[:, None] == got_col[None, :]).astype(jnp.bfloat16)
    chosen = jnp.dot(factors, pick, preferred_element_type=jnp.float32).astype(jnp.bfloat16)
    values = clenshaw(chosen, got_coeffs.astype(jnp.float32).T)

    total_sets = ns_cp.shape[0] * owners
    net_table = (got_ns[:, None] == jnp.arange(total_sets, dtype=jnp.int32)[None, :]).astype(
        jnp.bfloat16
    )
    netting = jnp.dot(values, net_table, preferred_element_type=jnp.float32)
    shares = lax.psum_scatter(netting, "trade", scatter_dimension=1, tiled=True)
    positive = jnp.maximum(shares, 0.0).astype(jnp.bfloat16)
    cp_table = (ns_cp[:, None] == jnp.arange(CP_DEV * owners, dtype=jnp.int32)[None, :]).astype(
        jnp.bfloat16
    )
    partial_cp = jnp.dot(positive, cp_table, preferred_element_type=jnp.float32)
    exposure = lax.psum_scatter(partial_cp, "trade", scatter_dimension=1, tiled=True).T
    return exposure


def solution(mesh):
    return jax.shard_map(
        per_device,
        mesh=mesh,
        in_specs=(
            P("path", None),
            P("path", "trade"),
            P("path", "trade"),
            P("trade", None),
            P("trade"),
            P("trade"),
            P("trade"),
        ),
        out_specs=P("trade", "path"),
        check_vma=False,
    )
```

```python
import jax
import jax.numpy as jnp
from jax import lax
from jax.sharding import Mesh, PartitionSpec as P

CP_DEV = 32


def clenshaw(chosen, coeffs_t):
    x = jnp.tanh(chosen.astype(jnp.float32) * 0.5)
    twice = x + x
    terms = coeffs_t.shape[0]
    b1 = jnp.zeros_like(x)
    b2 = jnp.zeros_like(x)
    for k in range(terms - 1, 0, -1):
        b1, b2 = coeffs_t[k][None, :] + twice * b1 - b2, b1
    return (coeffs_t[0][None, :] + x * b1 - b2).astype(jnp.bfloat16)


def regroup(trade_col, width, owners):
    count = trade_col.shape[0]
    per = count // owners
    block = trade_col // width
    onehot = (block[:, None] == jnp.arange(owners, dtype=jnp.int32)[None, :]).astype(jnp.bfloat16)
    lower = (
        jnp.arange(count, dtype=jnp.int32)[:, None] >= jnp.arange(count, dtype=jnp.int32)[None, :]
    ).astype(jnp.bfloat16)
    running = jnp.dot(lower, onehot, preferred_element_type=jnp.float32)
    rank = jnp.sum(running * onehot.astype(jnp.float32), axis=1).astype(jnp.int32) - 1
    slot = block * per + rank
    return (slot[:, None] == jnp.arange(count, dtype=jnp.int32)[None, :]).astype(jnp.float32)


def per_device(drivers, loadings, start_state, coeffs, trade_col, trade_ns, ns_cp):
    owners = lax.axis_size("trade")
    width = start_state.shape[1]
    count, terms = coeffs.shape
    per = count // owners

    place = regroup(trade_col, width, owners)
    offset = (trade_col % width).astype(jnp.float32)
    table = jnp.concatenate(
        [coeffs.astype(jnp.float32), offset[:, None], trade_ns.astype(jnp.float32)[:, None]], axis=1
    )
    sent = jnp.dot(place.T, table, precision=lax.Precision.HIGHEST)
    got = lax.all_to_all(sent.reshape(owners, per, terms + 2), "trade", 0, 0, tiled=False)
    got = got.reshape(count, terms + 2)
    got_coeffs = got[:, :terms].astype(jnp.bfloat16)
    got_col = got[:, terms].astype(jnp.int32)
    got_ns = got[:, terms + 1].astype(jnp.int32)

    gathered = lax.all_gather(loadings, "zh", axis=0, tiled=True)
    gathered = lax.all_gather(gathered, ("x", "y", "c"), axis=0, tiled=True)
    rows = drivers.shape[0]
    lead = loadings.shape[0]
    sizes = [lax.axis_size(name) for name in PATH]
    order = drivers.reshape(rows, *sizes, lead).transpose(0, 1, 3, 4, 2, 5).reshape(rows, -1)
    moved = jnp.dot(order, gathered, preferred_element_type=jnp.float32)
    factors = (start_state.astype(jnp.float32) + moved).astype(jnp.bfloat16)
    pick = (jnp.arange(width, dtype=jnp.int32)[:, None] == got_col[None, :]).astype(jnp.bfloat16)
    chosen = jnp.dot(factors, pick, preferred_element_type=jnp.float32).astype(jnp.bfloat16)
    values = clenshaw(chosen, got_coeffs.astype(jnp.float32).T)

    total_sets = ns_cp.shape[0] * owners
    net_table = (got_ns[:, None] == jnp.arange(total_sets, dtype=jnp.int32)[None, :]).astype(
        jnp.bfloat16
    )
    netting = jnp.dot(values, net_table, preferred_element_type=jnp.float32)
    shares = lax.psum_scatter(netting, "trade", scatter_dimension=1, tiled=True)
    positive = jnp.maximum(shares, 0.0).astype(jnp.bfloat16)
    cp_table = (ns_cp[:, None] == jnp.arange(CP_DEV * owners, dtype=jnp.int32)[None, :]).astype(
        jnp.bfloat16
    )
    partial_cp = jnp.dot(positive, cp_table, preferred_element_type=jnp.float32)
    pieces = lax.all_to_all(partial_cp.reshape(rows, owners, CP_DEV), "trade", 1, 1, tiled=False)
    return jnp.sum(pieces, axis=1).T


PATH = ("x", "zh", "y", "c")


def solution(mesh):
    fine = Mesh(mesh.devices.reshape(4, 2, 4, 2, -1), PATH + ("trade",))
    return jax.shard_map(
        per_device,
        mesh=fine,
        in_specs=(
            P(PATH, None),
            P(PATH, "trade"),
            P(PATH, "trade"),
            P("trade", None),
            P("trade"),
            P("trade"),
            P("trade"),
        ),
        out_specs=P("trade", PATH),
        check_vma=False,
    )
```

```python
import jax
import jax.numpy as jnp
from jax import lax
from jax.sharding import Mesh, PartitionSpec as P

CP_DEV = 32


def clenshaw(chosen, coeffs_t):
    x = jnp.tanh(chosen.astype(jnp.float32) * 0.5)
    twice = x + x
    terms = coeffs_t.shape[0]
    b1 = jnp.zeros_like(x)
    b2 = jnp.zeros_like(x)
    for k in range(terms - 1, 0, -1):
        b1, b2 = coeffs_t[k][None, :] + twice * b1 - b2, b1
    return (coeffs_t[0][None, :] + x * b1 - b2).astype(jnp.bfloat16)


def regroup(trade_col, width, owners):
    count = trade_col.shape[0]
    per = count // owners
    block = trade_col // width
    onehot = (block[:, None] == jnp.arange(owners, dtype=jnp.int32)[None, :]).astype(jnp.bfloat16)
    lower = (
        jnp.arange(count, dtype=jnp.int32)[:, None] >= jnp.arange(count, dtype=jnp.int32)[None, :]
    ).astype(jnp.bfloat16)
    running = jnp.dot(lower, onehot, preferred_element_type=jnp.float32)
    rank = jnp.sum(running * onehot.astype(jnp.float32), axis=1).astype(jnp.int32) - 1
    slot = block * per + rank
    return (slot[:, None] == jnp.arange(count, dtype=jnp.int32)[None, :]).astype(jnp.float32)


def ring_reduce(parts, owners):
    ring = list(range(0, owners, 2)) + list(range(owners - 1, 0, -2))
    where = [ring.index(t) for t in range(owners)]
    perm = [(ring[k], ring[(k + 1) % owners]) for k in range(owners)]
    here = jnp.asarray(where, jnp.int32)[lax.axis_index("trade")]
    ring_at = jnp.asarray(ring, jnp.int32)

    def own(step):
        owner = ring_at[(here - 1 - step) % owners]
        return lax.dynamic_index_in_dim(parts, owner, axis=1, keepdims=False)

    acc = own(0)
    for step in range(1, owners):
        acc = lax.ppermute(acc, "trade", perm) + own(step)
    return acc


def per_device(drivers, loadings, start_state, coeffs, trade_col, trade_ns, ns_cp):
    owners = lax.axis_size("trade")
    width = start_state.shape[1]
    count, terms = coeffs.shape
    per = count // owners

    place = regroup(trade_col, width, owners)
    offset = (trade_col % width).astype(jnp.float32)
    table = jnp.concatenate(
        [coeffs.astype(jnp.float32), offset[:, None], trade_ns.astype(jnp.float32)[:, None]], axis=1
    )
    sent = jnp.dot(place.T, table, precision=lax.Precision.HIGHEST)
    got = lax.all_to_all(sent.reshape(owners, per, terms + 2), "trade", 0, 0, tiled=False)
    got = got.reshape(count, terms + 2)
    got_coeffs = got[:, :terms].astype(jnp.bfloat16)
    got_col = got[:, terms].astype(jnp.int32)
    got_ns = got[:, terms + 1].astype(jnp.int32)

    gathered = lax.all_gather(loadings, "zh", axis=0, tiled=True)
    gathered = lax.all_gather(gathered, ("x", "y", "c"), axis=0, tiled=True)
    rows = drivers.shape[0]
    lead = loadings.shape[0]
    sizes = [lax.axis_size(name) for name in PATH]
    order = drivers.reshape(rows, *sizes, lead).transpose(0, 1, 3, 4, 2, 5).reshape(rows, -1)
    moved = jnp.dot(order, gathered, preferred_element_type=jnp.float32)
    factors = (start_state.astype(jnp.float32) + moved).astype(jnp.bfloat16)
    pick = (jnp.arange(width, dtype=jnp.int32)[:, None] == got_col[None, :]).astype(jnp.bfloat16)
    chosen = jnp.dot(factors, pick, preferred_element_type=jnp.float32).astype(jnp.bfloat16)
    values = clenshaw(chosen, got_coeffs.astype(jnp.float32).T)

    total_sets = ns_cp.shape[0] * owners
    net_table = (got_ns[:, None] == jnp.arange(total_sets, dtype=jnp.int32)[None, :]).astype(
        jnp.bfloat16
    )
    netting = jnp.dot(values, net_table, preferred_element_type=jnp.float32)
    shares = ring_reduce(netting.reshape(rows, owners, -1), owners)
    positive = jnp.maximum(shares, 0.0).astype(jnp.bfloat16)
    cp_table = (ns_cp[:, None] == jnp.arange(CP_DEV * owners, dtype=jnp.int32)[None, :]).astype(
        jnp.bfloat16
    )
    partial_cp = jnp.dot(positive, cp_table, preferred_element_type=jnp.float32)
    pieces = lax.all_to_all(partial_cp.reshape(rows, owners, CP_DEV), "trade", 1, 1, tiled=False)
    return jnp.sum(pieces, axis=1).T


PATH = ("x", "zh", "y", "c")


def solution(mesh):
    fine = Mesh(mesh.devices.reshape(4, 2, 4, 2, -1), PATH + ("trade",))
    return jax.shard_map(
        per_device,
        mesh=fine,
        in_specs=(
            P(PATH, None),
            P(PATH, "trade"),
            P(PATH, "trade"),
            P("trade", None),
            P("trade"),
            P("trade"),
            P("trade"),
        ),
        out_specs=P("trade", PATH),
        check_vma=False,
    )
```

```python
import jax
import jax.numpy as jnp
from jax import lax
from jax.sharding import Mesh, PartitionSpec as P

CP_DEV = 32


def clenshaw(chosen, coeffs_t):
    x = jnp.tanh(chosen.astype(jnp.float32) * 0.5)
    twice = x + x
    terms = coeffs_t.shape[0]
    b1 = jnp.zeros_like(x)
    b2 = jnp.zeros_like(x)
    for k in range(terms - 1, 0, -1):
        b1, b2 = coeffs_t[k][None, :] + twice * b1 - b2, b1
    return (coeffs_t[0][None, :] + x * b1 - b2).astype(jnp.bfloat16)


def regroup(trade_col, width, owners):
    count = trade_col.shape[0]
    per = count // owners
    block = trade_col // width
    onehot = (block[:, None] == jnp.arange(owners, dtype=jnp.int32)[None, :]).astype(jnp.bfloat16)
    lower = (
        jnp.arange(count, dtype=jnp.int32)[:, None] >= jnp.arange(count, dtype=jnp.int32)[None, :]
    ).astype(jnp.bfloat16)
    running = jnp.dot(lower, onehot, preferred_element_type=jnp.float32)
    rank = jnp.sum(running * onehot.astype(jnp.float32), axis=1).astype(jnp.int32) - 1
    slot = block * per + rank
    return (slot[:, None] == jnp.arange(count, dtype=jnp.int32)[None, :]).astype(jnp.float32)


def ring_reduce(parts, owners):
    ring = list(range(0, owners, 2)) + list(range(owners - 1, 0, -2))
    where = [ring.index(t) for t in range(owners)]
    perm = [(ring[k], ring[(k + 1) % owners]) for k in range(owners)]
    here = jnp.asarray(where, jnp.int32)[lax.axis_index("trade")]
    ring_at = jnp.asarray(ring, jnp.int32)

    def own(step):
        owner = ring_at[(here - 1 - step) % owners]
        return lax.dynamic_index_in_dim(parts, owner, axis=1, keepdims=False)

    acc = own(0)
    for step in range(1, owners):
        acc = lax.ppermute(acc, "trade", perm) + own(step)
    return acc


def per_device(drivers, loadings, start_state, coeffs, trade_col, trade_ns, ns_cp):
    owners = lax.axis_size("trade")
    width = start_state.shape[1]
    count, terms = coeffs.shape
    per = count // owners

    place = regroup(trade_col, width, owners)
    offset = (trade_col % width).astype(jnp.float32)
    table = jnp.concatenate(
        [coeffs.astype(jnp.float32), offset[:, None], trade_ns.astype(jnp.float32)[:, None]], axis=1
    )
    sent = jnp.dot(place.T, table, precision=lax.Precision.HIGHEST)
    got = lax.all_to_all(sent.reshape(owners, per, terms + 2), "trade", 0, 0, tiled=False)
    got = got.reshape(count, terms + 2)
    got_coeffs = got[:, :terms].astype(jnp.bfloat16)
    got_col = got[:, terms].astype(jnp.int32)
    got_ns = got[:, terms + 1].astype(jnp.int32)

    gathered = lax.all_gather(loadings, "zh", axis=0, tiled=True)
    gathered = lax.all_gather(gathered, ("x", "y", "c"), axis=0, tiled=True)
    rows = drivers.shape[0]
    lead = loadings.shape[0]
    sizes = [lax.axis_size(name) for name in PATH]
    order = drivers.reshape(rows, *sizes, lead).transpose(0, 1, 3, 4, 2, 5).reshape(rows, -1)
    moved = jnp.dot(order, gathered, preferred_element_type=jnp.float32)
    factors = (start_state.astype(jnp.float32) + moved).astype(jnp.bfloat16)
    pick = (jnp.arange(width, dtype=jnp.int32)[:, None] == got_col[None, :]).astype(jnp.bfloat16)
    chosen = jnp.dot(factors, pick, preferred_element_type=jnp.float32).astype(jnp.bfloat16)
    values = clenshaw(chosen, got_coeffs.astype(jnp.float32).T)

    total_sets = ns_cp.shape[0] * owners
    net_table = (got_ns[:, None] == jnp.arange(total_sets, dtype=jnp.int32)[None, :]).astype(
        jnp.bfloat16
    )
    netting = jnp.dot(values, net_table, preferred_element_type=jnp.float32)
    shares = jnp.sum(lax.all_to_all(netting.reshape(rows, owners, -1), "trade", 1, 1, tiled=False), axis=1)
    positive = jnp.maximum(shares, 0.0).astype(jnp.bfloat16)
    cp_table = (ns_cp[:, None] == jnp.arange(CP_DEV * owners, dtype=jnp.int32)[None, :]).astype(
        jnp.bfloat16
    )
    partial_cp = jnp.dot(positive, cp_table, preferred_element_type=jnp.float32)
    pieces = lax.all_to_all(partial_cp.reshape(rows, owners, CP_DEV), "trade", 1, 1, tiled=False)
    return jnp.sum(pieces, axis=1).T


PATH = ("x", "zh", "y", "c")


def solution(mesh):
    fine = Mesh(mesh.devices.reshape(4, 2, 4, 2, -1), PATH + ("trade",))
    return jax.shard_map(
        per_device,
        mesh=fine,
        in_specs=(
            P(PATH, None),
            P(PATH, "trade"),
            P(PATH, "trade"),
            P("trade", None),
            P("trade"),
            P("trade"),
            P("trade"),
        ),
        out_specs=P("trade", PATH),
        check_vma=False,
    )
```

```python
import jax
import jax.numpy as jnp
from jax import lax
from jax.sharding import Mesh, PartitionSpec as P

CP_DEV = 32


def clenshaw(chosen, coeffs_t):
    x = jnp.tanh(chosen.astype(jnp.float32) * 0.5)
    twice = x + x
    terms = coeffs_t.shape[0]
    b1 = jnp.zeros_like(x)
    b2 = jnp.zeros_like(x)
    for k in range(terms - 1, 0, -1):
        b1, b2 = coeffs_t[k][None, :] + twice * b1 - b2, b1
    return (coeffs_t[0][None, :] + x * b1 - b2).astype(jnp.bfloat16)


def regroup(trade_col, width, owners):
    count = trade_col.shape[0]
    per = count // owners
    block = trade_col // width
    onehot = (block[:, None] == jnp.arange(owners, dtype=jnp.int32)[None, :]).astype(jnp.bfloat16)
    lower = (
        jnp.arange(count, dtype=jnp.int32)[:, None] >= jnp.arange(count, dtype=jnp.int32)[None, :]
    ).astype(jnp.bfloat16)
    running = jnp.dot(lower, onehot, preferred_element_type=jnp.float32)
    rank = jnp.sum(running * onehot.astype(jnp.float32), axis=1).astype(jnp.int32) - 1
    slot = block * per + rank
    return (slot[:, None] == jnp.arange(count, dtype=jnp.int32)[None, :]).astype(jnp.float32)


def ring_reduce(parts, owners):
    ring = list(range(0, owners, 2)) + list(range(owners - 1, 0, -2))
    where = [ring.index(t) for t in range(owners)]
    perm = [(ring[k], ring[(k + 1) % owners]) for k in range(owners)]
    here = jnp.asarray(where, jnp.int32)[lax.axis_index("trade")]
    ring_at = jnp.asarray(ring, jnp.int32)

    def own(step):
        owner = ring_at[(here - 1 - step) % owners]
        return lax.dynamic_index_in_dim(parts, owner, axis=1, keepdims=False)

    acc = own(0)
    for step in range(1, owners):
        acc = lax.ppermute(acc, "trade", perm) + own(step)
    return acc


def per_device(drivers, loadings, start_state, coeffs, trade_col, trade_ns, ns_cp):
    owners = lax.axis_size("trade")
    width = start_state.shape[1]
    count, terms = coeffs.shape
    per = count // owners

    place = regroup(trade_col, width, owners)
    offset = (trade_col % width).astype(jnp.float32)
    table = jnp.concatenate(
        [coeffs.astype(jnp.float32), offset[:, None], trade_ns.astype(jnp.float32)[:, None]], axis=1
    )
    sent = jnp.dot(place.T, table, precision=lax.Precision.HIGHEST)
    got = lax.all_to_all(sent.reshape(owners, per, terms + 2), "trade", 0, 0, tiled=False)
    got = got.reshape(count, terms + 2)
    got_coeffs = got[:, :terms].astype(jnp.bfloat16)
    got_col = got[:, terms].astype(jnp.int32)
    got_ns = got[:, terms + 1].astype(jnp.int32)

    gathered = lax.all_gather(loadings, "zh", axis=0, tiled=True)
    gathered = lax.all_gather(gathered, ("x", "y", "c"), axis=0, tiled=True)
    rows = drivers.shape[0]
    lead = loadings.shape[0]
    sizes = [lax.axis_size(name) for name in PATH]
    order = drivers.reshape(rows, *sizes, lead).transpose(0, 1, 3, 4, 2, 5).reshape(rows, -1)
    moved = jnp.dot(order, gathered, preferred_element_type=jnp.float32)
    factors = (start_state.astype(jnp.float32) + moved).astype(jnp.bfloat16)
    pick = (jnp.arange(width, dtype=jnp.int32)[:, None] == got_col[None, :]).astype(jnp.bfloat16)
    chosen = jnp.dot(factors, pick, preferred_element_type=jnp.float32).astype(jnp.bfloat16)
    values = clenshaw(chosen, got_coeffs.astype(jnp.float32).T)

    total_sets = ns_cp.shape[0] * owners
    net_table = (got_ns[:, None] == jnp.arange(total_sets, dtype=jnp.int32)[None, :]).astype(
        jnp.bfloat16
    )
    netting = jnp.dot(values, net_table, preferred_element_type=jnp.float32)
    sent = netting.astype(jnp.bfloat16).reshape(rows, owners, -1)
    shares = jnp.sum(lax.all_to_all(sent, "trade", 1, 1, tiled=False).astype(jnp.float32), axis=1)
    positive = jnp.maximum(shares, 0.0).astype(jnp.bfloat16)
    cp_table = (ns_cp[:, None] == jnp.arange(CP_DEV * owners, dtype=jnp.int32)[None, :]).astype(
        jnp.bfloat16
    )
    partial_cp = jnp.dot(positive, cp_table, preferred_element_type=jnp.float32)
    pieces = lax.all_to_all(partial_cp.reshape(rows, owners, CP_DEV), "trade", 1, 1, tiled=False)
    return jnp.sum(pieces, axis=1).T


PATH = ("x", "zh", "y", "c")


def solution(mesh):
    fine = Mesh(mesh.devices.reshape(4, 2, 4, 2, -1), PATH + ("trade",))
    return jax.shard_map(
        per_device,
        mesh=fine,
        in_specs=(
            P(PATH, None),
            P(PATH, "trade"),
            P(PATH, "trade"),
            P("trade", None),
            P("trade"),
            P("trade"),
            P("trade"),
        ),
        out_specs=P("trade", PATH),
        check_vma=False,
    )
```

```python
import jax
import jax.numpy as jnp
from jax import lax
from jax.sharding import Mesh, PartitionSpec as P

CP_DEV = 32


def clenshaw(chosen, coeffs_t):
    x = jnp.tanh(chosen.astype(jnp.float32) * 0.5)
    twice = x + x
    terms = coeffs_t.shape[0]
    b1 = jnp.zeros_like(x)
    b2 = jnp.zeros_like(x)
    for k in range(terms - 1, 0, -1):
        b1, b2 = coeffs_t[k][None, :] + twice * b1 - b2, b1
    return (coeffs_t[0][None, :] + x * b1 - b2).astype(jnp.bfloat16)


def regroup(trade_col, width, owners):
    count = trade_col.shape[0]
    per = count // owners
    block = trade_col // width
    onehot = (block[:, None] == jnp.arange(owners, dtype=jnp.int32)[None, :]).astype(jnp.bfloat16)
    lower = (
        jnp.arange(count, dtype=jnp.int32)[:, None] >= jnp.arange(count, dtype=jnp.int32)[None, :]
    ).astype(jnp.bfloat16)
    running = jnp.dot(lower, onehot, preferred_element_type=jnp.float32)
    rank = jnp.sum(running * onehot.astype(jnp.float32), axis=1).astype(jnp.int32) - 1
    slot = block * per + rank
    return (slot[:, None] == jnp.arange(count, dtype=jnp.int32)[None, :]).astype(jnp.float32)


def ring_reduce(parts, owners):
    ring = list(range(0, owners, 2)) + list(range(owners - 1, 0, -2))
    where = [ring.index(t) for t in range(owners)]
    perm = [(ring[k], ring[(k + 1) % owners]) for k in range(owners)]
    here = jnp.asarray(where, jnp.int32)[lax.axis_index("trade")]
    ring_at = jnp.asarray(ring, jnp.int32)

    def own(step):
        owner = ring_at[(here - 1 - step) % owners]
        return lax.dynamic_index_in_dim(parts, owner, axis=1, keepdims=False)

    acc = own(0)
    for step in range(1, owners):
        acc = lax.ppermute(acc, "trade", perm) + own(step)
    return acc


def per_device(drivers, loadings, start_state, coeffs, trade_col, trade_ns, ns_cp):
    owners = lax.axis_size("trade")
    width = start_state.shape[1]
    count, terms = coeffs.shape
    per = count // owners

    place = regroup(trade_col, width, owners)
    offset = (trade_col % width).astype(jnp.float32)
    table = jnp.concatenate(
        [coeffs.astype(jnp.float32), offset[:, None], trade_ns.astype(jnp.float32)[:, None]], axis=1
    )
    sent = jnp.dot(place.T, table, precision=lax.Precision.HIGHEST)
    got = lax.all_to_all(sent.reshape(owners, per, terms + 2), "trade", 0, 0, tiled=False)
    got = got.reshape(count, terms + 2)
    got_coeffs = got[:, :terms].astype(jnp.bfloat16)
    got_col = got[:, terms].astype(jnp.int32)
    got_ns = got[:, terms + 1].astype(jnp.int32)

    rows = drivers.shape[0]
    lead = loadings.shape[0]
    sizes = [lax.axis_size(name) for name in PATH]
    cores = sizes[3]
    half = width // cores
    mine = lax.all_to_all(loadings.reshape(lead, cores, half), "c", 1, 0, tiled=False)
    gathered = lax.all_gather(mine.reshape(cores * lead, half), "zh", axis=0, tiled=True)
    gathered = lax.all_gather(gathered, ("x", "y"), axis=0, tiled=True)
    both = lax.all_gather(drivers, "c", axis=0, tiled=True)
    order = both.reshape(cores * rows, *sizes, lead).transpose(0, 1, 3, 2, 4, 5).reshape(cores * rows, -1)
    moved = jnp.dot(order, gathered, preferred_element_type=jnp.float32)
    before = lax.all_to_all(start_state.reshape(rows, cores, half), "c", 1, 0, tiled=False)
    halves = (before.reshape(cores * rows, half).astype(jnp.float32) + moved).astype(jnp.bfloat16)
    back = lax.all_to_all(halves.reshape(cores, rows, half), "c", 0, 1, tiled=False)
    factors = back.reshape(rows, width)
    pick = (jnp.arange(width, dtype=jnp.int32)[:, None] == got_col[None, :]).astype(jnp.bfloat16)
    chosen = jnp.dot(factors, pick, preferred_element_type=jnp.float32).astype(jnp.bfloat16)
    values = clenshaw(chosen, got_coeffs.astype(jnp.float32).T)

    total_sets = ns_cp.shape[0] * owners
    net_table = (got_ns[:, None] == jnp.arange(total_sets, dtype=jnp.int32)[None, :]).astype(
        jnp.bfloat16
    )
    netting = jnp.dot(values, net_table, preferred_element_type=jnp.float32)
    sent = netting.astype(jnp.bfloat16).reshape(rows, owners, -1)
    shares = jnp.sum(lax.all_to_all(sent, "trade", 1, 1, tiled=False).astype(jnp.float32), axis=1)
    positive = jnp.maximum(shares, 0.0).astype(jnp.bfloat16)
    cp_table = (ns_cp[:, None] == jnp.arange(CP_DEV * owners, dtype=jnp.int32)[None, :]).astype(
        jnp.bfloat16
    )
    partial_cp = jnp.dot(positive, cp_table, preferred_element_type=jnp.float32)
    pieces = lax.all_to_all(partial_cp.reshape(rows, owners, CP_DEV), "trade", 1, 1, tiled=False)
    return jnp.sum(pieces, axis=1).T


PATH = ("x", "zh", "y", "c")


def solution(mesh):
    fine = Mesh(mesh.devices.reshape(4, 2, 4, 2, -1), PATH + ("trade",))
    return jax.shard_map(
        per_device,
        mesh=fine,
        in_specs=(
            P(PATH, None),
            P(PATH, "trade"),
            P(PATH, "trade"),
            P("trade", None),
            P("trade"),
            P("trade"),
            P("trade"),
        ),
        out_specs=P("trade", PATH),
        check_vma=False,
    )
```

```python
import jax
import jax.numpy as jnp
from jax import lax
from jax.sharding import Mesh, PartitionSpec as P

CP_DEV = 32


def clenshaw(chosen, coeffs_t):
    x = jnp.tanh(chosen.astype(jnp.float32) * 0.5)
    twice = x + x
    terms = coeffs_t.shape[0]
    b1 = jnp.zeros_like(x)
    b2 = jnp.zeros_like(x)
    for k in range(terms - 1, 0, -1):
        b1, b2 = coeffs_t[k][None, :] + twice * b1 - b2, b1
    return (coeffs_t[0][None, :] + x * b1 - b2).astype(jnp.bfloat16)


def regroup(trade_col, width, owners):
    count = trade_col.shape[0]
    per = count // owners
    block = trade_col // width
    onehot = (block[:, None] == jnp.arange(owners, dtype=jnp.int32)[None, :]).astype(jnp.bfloat16)
    lower = (
        jnp.arange(count, dtype=jnp.int32)[:, None] >= jnp.arange(count, dtype=jnp.int32)[None, :]
    ).astype(jnp.bfloat16)
    running = jnp.dot(lower, onehot, preferred_element_type=jnp.float32)
    rank = jnp.sum(running * onehot.astype(jnp.float32), axis=1).astype(jnp.int32) - 1
    slot = block * per + rank
    return (slot[:, None] == jnp.arange(count, dtype=jnp.int32)[None, :]).astype(jnp.float32)


def ring_reduce(parts, owners):
    ring = list(range(0, owners, 2)) + list(range(owners - 1, 0, -2))
    where = [ring.index(t) for t in range(owners)]
    perm = [(ring[k], ring[(k + 1) % owners]) for k in range(owners)]
    here = jnp.asarray(where, jnp.int32)[lax.axis_index("trade")]
    ring_at = jnp.asarray(ring, jnp.int32)

    def own(step):
        owner = ring_at[(here - 1 - step) % owners]
        return lax.dynamic_index_in_dim(parts, owner, axis=1, keepdims=False)

    acc = own(0)
    for step in range(1, owners):
        acc = lax.ppermute(acc, "trade", perm) + own(step)
    return acc


def per_device(drivers, loadings, start_state, coeffs, trade_col, trade_ns, ns_cp):
    owners = lax.axis_size("trade")
    width = start_state.shape[1]
    count, terms = coeffs.shape
    per = count // owners

    place = regroup(trade_col, width, owners)
    offset = (trade_col % width).astype(jnp.float32)
    table = jnp.concatenate(
        [coeffs.astype(jnp.float32), offset[:, None], trade_ns.astype(jnp.float32)[:, None]], axis=1
    )
    sent = jnp.dot(place.T, table, precision=lax.Precision.HIGHEST)
    got = lax.all_to_all(sent.reshape(owners, per, terms + 2), "trade", 0, 0, tiled=False)
    got = got.reshape(count, terms + 2)
    got_coeffs = got[:, :terms].astype(jnp.bfloat16)
    got_col = got[:, terms].astype(jnp.int32)
    got_ns = got[:, terms + 1].astype(jnp.int32)

    gathered = lax.all_gather(loadings, "zh", axis=0, tiled=True)
    gathered = lax.all_gather(gathered, ("x", "y", "c"), axis=0, tiled=True)
    rows = drivers.shape[0]
    lead = loadings.shape[0]
    sizes = [lax.axis_size(name) for name in PATH]
    order = drivers.reshape(rows, *sizes, lead).transpose(0, 1, 3, 4, 2, 5).reshape(rows, -1)
    moved = jnp.dot(order, gathered, preferred_element_type=jnp.float32)
    factors = (start_state.astype(jnp.float32) + moved).astype(jnp.bfloat16)
    pick = (jnp.arange(width, dtype=jnp.int32)[:, None] == got_col[None, :]).astype(jnp.bfloat16)
    chosen = jnp.dot(factors, pick, preferred_element_type=jnp.float32).astype(jnp.bfloat16)
    values = clenshaw(chosen, got_coeffs.astype(jnp.float32).T)

    total_sets = ns_cp.shape[0] * owners
    net_table = (got_ns[:, None] == jnp.arange(total_sets, dtype=jnp.int32)[None, :]).astype(
        jnp.bfloat16
    )
    netting = jnp.dot(values, net_table, preferred_element_type=jnp.float32)
    sent = netting.astype(jnp.bfloat16).reshape(rows, owners, -1)
    shares = jnp.sum(lax.all_to_all(sent, "trade", 1, 1, tiled=False).astype(jnp.float32), axis=1)
    positive = jnp.maximum(shares, 0.0).astype(jnp.bfloat16)
    cp_table = (ns_cp[:, None] == jnp.arange(CP_DEV * owners, dtype=jnp.int32)[None, :]).astype(
        jnp.bfloat16
    )
    partial_cp = jnp.dot(positive, cp_table, preferred_element_type=jnp.float32)
    sent_cp = partial_cp.astype(jnp.bfloat16).reshape(rows, owners, CP_DEV)
    pieces = lax.all_to_all(sent_cp, "trade", 1, 1, tiled=False).astype(jnp.float32)
    return jnp.sum(pieces, axis=1).T


PATH = ("x", "zh", "y", "c")


def solution(mesh):
    fine = Mesh(mesh.devices.reshape(4, 2, 4, 2, -1), PATH + ("trade",))
    return jax.shard_map(
        per_device,
        mesh=fine,
        in_specs=(
            P(PATH, None),
            P(PATH, "trade"),
            P(PATH, "trade"),
            P("trade", None),
            P("trade"),
            P("trade"),
            P("trade"),
        ),
        out_specs=P("trade", PATH),
        check_vma=False,
    )
```

```python
import jax
import jax.numpy as jnp
from jax import lax
from jax.sharding import Mesh, PartitionSpec as P

CP_DEV = 32


def clenshaw(chosen, coeffs_t):
    x = jnp.tanh(chosen.astype(jnp.float32) * 0.5)
    twice = x + x
    terms = coeffs_t.shape[0]
    b1 = jnp.zeros_like(x)
    b2 = jnp.zeros_like(x)
    for k in range(terms - 1, 0, -1):
        b1, b2 = coeffs_t[k][None, :] + twice * b1 - b2, b1
    return (coeffs_t[0][None, :] + x * b1 - b2).astype(jnp.bfloat16)


def regroup(trade_col, width, owners):
    count = trade_col.shape[0]
    per = count // owners
    block = trade_col // width
    onehot = (block[:, None] == jnp.arange(owners, dtype=jnp.int32)[None, :]).astype(jnp.bfloat16)
    lower = (
        jnp.arange(count, dtype=jnp.int32)[:, None] >= jnp.arange(count, dtype=jnp.int32)[None, :]
    ).astype(jnp.bfloat16)
    running = jnp.dot(lower, onehot, preferred_element_type=jnp.float32)
    rank = jnp.sum(running * onehot.astype(jnp.float32), axis=1).astype(jnp.int32) - 1
    slot = block * per + rank
    return (slot[:, None] == jnp.arange(count, dtype=jnp.int32)[None, :]).astype(jnp.float32)


def ring_reduce(parts, owners):
    ring = list(range(0, owners, 2)) + list(range(owners - 1, 0, -2))
    where = [ring.index(t) for t in range(owners)]
    perm = [(ring[k], ring[(k + 1) % owners]) for k in range(owners)]
    here = jnp.asarray(where, jnp.int32)[lax.axis_index("trade")]
    ring_at = jnp.asarray(ring, jnp.int32)

    def own(step):
        owner = ring_at[(here - 1 - step) % owners]
        return lax.dynamic_index_in_dim(parts, owner, axis=1, keepdims=False)

    acc = own(0)
    for step in range(1, owners):
        acc = lax.ppermute(acc, "trade", perm) + own(step)
    return acc


def across_planes(block):
    planes = lax.axis_size("zh")
    owners = lax.axis_size("trade")
    ring = planes * owners
    split = block.shape[1] // 2
    straight = lax.ppermute(block[:, :split], "zh", [(z, (z + 1) % planes) for z in range(planes)])
    back = [(z, (z - ring // 4) % ring) for z in range(ring)]
    relayed = lax.ppermute(lax.ppermute(block[:, split:], ("zh", "trade"), back), ("zh", "trade"), back)
    partner = jnp.concatenate([straight, relayed], axis=1)
    first = lax.axis_index("zh") == 0
    return jnp.where(first, jnp.concatenate([block, partner]), jnp.concatenate([partner, block]))


def per_device(drivers, loadings, start_state, coeffs, trade_col, trade_ns, ns_cp):
    owners = lax.axis_size("trade")
    width = start_state.shape[1]
    count, terms = coeffs.shape
    per = count // owners

    place = regroup(trade_col, width, owners)
    offset = (trade_col % width).astype(jnp.float32)
    table = jnp.concatenate(
        [coeffs.astype(jnp.float32), offset[:, None], trade_ns.astype(jnp.float32)[:, None]], axis=1
    )
    sent = jnp.dot(place.T, table, precision=lax.Precision.HIGHEST)
    got = lax.all_to_all(sent.reshape(owners, per, terms + 2), "trade", 0, 0, tiled=False)
    got = got.reshape(count, terms + 2)
    got_coeffs = got[:, :terms].astype(jnp.bfloat16)
    got_col = got[:, terms].astype(jnp.int32)
    got_ns = got[:, terms + 1].astype(jnp.int32)

    gathered = across_planes(loadings)
    gathered = lax.all_gather(gathered, ("x", "y", "c"), axis=0, tiled=True)
    rows = drivers.shape[0]
    lead = loadings.shape[0]
    sizes = [lax.axis_size(name) for name in PATH]
    order = drivers.reshape(rows, *sizes, lead).transpose(0, 1, 3, 4, 2, 5).reshape(rows, -1)
    moved = jnp.dot(order, gathered, preferred_element_type=jnp.float32)
    factors = (start_state.astype(jnp.float32) + moved).astype(jnp.bfloat16)
    pick = (jnp.arange(width, dtype=jnp.int32)[:, None] == got_col[None, :]).astype(jnp.bfloat16)
    chosen = jnp.dot(factors, pick, preferred_element_type=jnp.float32).astype(jnp.bfloat16)
    values = clenshaw(chosen, got_coeffs.astype(jnp.float32).T)

    total_sets = ns_cp.shape[0] * owners
    net_table = (got_ns[:, None] == jnp.arange(total_sets, dtype=jnp.int32)[None, :]).astype(
        jnp.bfloat16
    )
    netting = jnp.dot(values, net_table, preferred_element_type=jnp.float32)
    sent = netting.astype(jnp.bfloat16).reshape(rows, owners, -1)
    shares = jnp.sum(lax.all_to_all(sent, "trade", 1, 1, tiled=False).astype(jnp.float32), axis=1)
    positive = jnp.maximum(shares, 0.0).astype(jnp.bfloat16)
    cp_table = (ns_cp[:, None] == jnp.arange(CP_DEV * owners, dtype=jnp.int32)[None, :]).astype(
        jnp.bfloat16
    )
    partial_cp = jnp.dot(positive, cp_table, preferred_element_type=jnp.float32)
    pieces = lax.all_to_all(partial_cp.reshape(rows, owners, CP_DEV), "trade", 1, 1, tiled=False)
    return jnp.sum(pieces, axis=1).T


PATH = ("x", "zh", "y", "c")


def solution(mesh):
    fine = Mesh(mesh.devices.reshape(4, 2, 4, 2, -1), PATH + ("trade",))
    return jax.shard_map(
        per_device,
        mesh=fine,
        in_specs=(
            P(PATH, None),
            P(PATH, "trade"),
            P(PATH, "trade"),
            P("trade", None),
            P("trade"),
            P("trade"),
            P("trade"),
        ),
        out_specs=P("trade", PATH),
        check_vma=False,
    )
```

```python
import jax
import jax.numpy as jnp
from jax import lax
from jax.sharding import Mesh, PartitionSpec as P

CP_DEV = 32
ROOM = 304


def clenshaw(chosen, coeffs_t):
    x = jnp.tanh(chosen.astype(jnp.float32) * 0.5)
    twice = x + x
    terms = coeffs_t.shape[0]
    b1 = jnp.zeros_like(x)
    b2 = jnp.zeros_like(x)
    for k in range(terms - 1, 0, -1):
        b1, b2 = coeffs_t[k][None, :] + twice * b1 - b2, b1
    return (coeffs_t[0][None, :] + x * b1 - b2).astype(jnp.bfloat16)


def regroup(trade_col, width, owners):
    count = trade_col.shape[0]
    per = count // owners
    block = trade_col // width
    onehot = (block[:, None] == jnp.arange(owners, dtype=jnp.int32)[None, :]).astype(jnp.bfloat16)
    lower = (
        jnp.arange(count, dtype=jnp.int32)[:, None] >= jnp.arange(count, dtype=jnp.int32)[None, :]
    ).astype(jnp.bfloat16)
    running = jnp.dot(lower, onehot, preferred_element_type=jnp.float32)
    rank = jnp.sum(running * onehot.astype(jnp.float32), axis=1).astype(jnp.int32) - 1
    slot = block * per + rank
    return (slot[:, None] == jnp.arange(count, dtype=jnp.int32)[None, :]).astype(jnp.float32)


def ring_reduce(parts, owners):
    ring = list(range(0, owners, 2)) + list(range(owners - 1, 0, -2))
    where = [ring.index(t) for t in range(owners)]
    perm = [(ring[k], ring[(k + 1) % owners]) for k in range(owners)]
    here = jnp.asarray(where, jnp.int32)[lax.axis_index("trade")]
    ring_at = jnp.asarray(ring, jnp.int32)

    def own(step):
        owner = ring_at[(here - 1 - step) % owners]
        return lax.dynamic_index_in_dim(parts, owner, axis=1, keepdims=False)

    acc = own(0)
    for step in range(1, owners):
        acc = lax.ppermute(acc, "trade", perm) + own(step)
    return acc


def per_device(drivers, loadings, start_state, coeffs, trade_col, trade_ns, ns_cp):
    owners = lax.axis_size("trade")
    width = start_state.shape[1]
    count, terms = coeffs.shape
    per = count // owners

    place = regroup(trade_col, width, owners)
    offset = (trade_col % width).astype(jnp.float32)
    table = jnp.concatenate(
        [coeffs.astype(jnp.float32), offset[:, None], trade_ns.astype(jnp.float32)[:, None]], axis=1
    )
    sent = jnp.dot(place.T, table, precision=lax.Precision.HIGHEST)
    sets = ns_cp.shape[0]
    spread = jnp.broadcast_to(ns_cp.astype(jnp.float32).reshape(sets // per, per).T, (owners, per, sets // per))
    sent = jnp.concatenate([sent.reshape(owners, per, terms + 2), spread], axis=2)
    got = lax.all_to_all(sent, "trade", 0, 0, tiled=False)
    all_cp = got[:, :, terms + 2 :].transpose(0, 2, 1).reshape(owners * sets).astype(jnp.int32)
    got = got[:, :, : terms + 2].reshape(count, terms + 2)
    got_coeffs = got[:, :terms].astype(jnp.bfloat16)
    got_col = got[:, terms].astype(jnp.int32)
    got_ns = got[:, terms + 1].astype(jnp.int32)

    gathered = lax.all_gather(loadings, "zh", axis=0, tiled=True)
    gathered = lax.all_gather(gathered, ("x", "y", "c"), axis=0, tiled=True)
    rows = drivers.shape[0]
    lead = loadings.shape[0]
    sizes = [lax.axis_size(name) for name in PATH]
    order = drivers.reshape(rows, *sizes, lead).transpose(0, 1, 3, 4, 2, 5).reshape(rows, -1)
    moved = jnp.dot(order, gathered, preferred_element_type=jnp.float32)
    factors = (start_state.astype(jnp.float32) + moved).astype(jnp.bfloat16)
    pick = (jnp.arange(width, dtype=jnp.int32)[:, None] == got_col[None, :]).astype(jnp.bfloat16)
    chosen = jnp.dot(factors, pick, preferred_element_type=jnp.float32).astype(jnp.bfloat16)
    values = clenshaw(chosen, got_coeffs.astype(jnp.float32).T)

    def by_set_owner(values):
        total_sets = sets * owners
        net_table = (got_ns[:, None] == jnp.arange(total_sets, dtype=jnp.int32)[None, :]).astype(
            jnp.bfloat16
        )
        netting = jnp.dot(values, net_table, preferred_element_type=jnp.float32)
        sent = netting.astype(jnp.bfloat16).reshape(rows, owners, -1)
        shares = jnp.sum(lax.all_to_all(sent, "trade", 1, 1, tiled=False).astype(jnp.float32), axis=1)
        positive = jnp.maximum(shares, 0.0).astype(jnp.bfloat16)
        cp_table = (ns_cp[:, None] == jnp.arange(CP_DEV * owners, dtype=jnp.int32)[None, :]).astype(
            jnp.bfloat16
        )
        partial_cp = jnp.dot(positive, cp_table, preferred_element_type=jnp.float32)
        pieces = lax.all_to_all(partial_cp.reshape(rows, owners, CP_DEV), "trade", 1, 1, tiled=False)
        return jnp.sum(pieces, axis=1).T

    total_sets = sets * owners
    boss = all_cp // CP_DEV
    mask = (boss[:, None] == jnp.arange(owners, dtype=jnp.int32)[None, :]).astype(jnp.bfloat16)
    lower = (
        jnp.arange(total_sets, dtype=jnp.int32)[:, None] >= jnp.arange(total_sets, dtype=jnp.int32)[None, :]
    ).astype(jnp.bfloat16)
    running = jnp.dot(lower, mask, preferred_element_type=jnp.float32)
    rank = jnp.sum(running * mask.astype(jnp.float32), axis=1).astype(jnp.int32) - 1
    fits = jnp.max(rank) < ROOM
    slot = boss * ROOM + rank

    def by_cp_owner(values):
        trade_slot = jnp.take(slot, got_ns)
        route = (trade_slot[None, :] == jnp.arange(owners * ROOM, dtype=jnp.int32)[:, None]).astype(
            jnp.bfloat16
        )
        routed = lax.dot_general(
            route, values, (((1,), (1,)), ((), ())), preferred_element_type=jnp.float32
        )
        sent = routed.astype(jnp.bfloat16).reshape(owners, ROOM, rows)
        netting = jnp.sum(lax.all_to_all(sent, "trade", 0, 0, tiled=False).astype(jnp.float32), axis=0)
        positive = jnp.maximum(netting, 0.0).astype(jnp.bfloat16)
        here = lax.axis_index("trade")
        at_slot = (
            (boss[:, None] == here) & (rank[:, None] == jnp.arange(ROOM, dtype=jnp.int32)[None, :])
        ).astype(jnp.bfloat16)
        of_cp = (
            all_cp[:, None] == here * CP_DEV + jnp.arange(CP_DEV, dtype=jnp.int32)[None, :]
        ).astype(jnp.bfloat16)
        cp_table = lax.dot_general(
            of_cp, at_slot, (((0,), (0,)), ((), ())), preferred_element_type=jnp.float32
        ).astype(jnp.bfloat16)
        return jnp.dot(cp_table, positive, preferred_element_type=jnp.float32)

    return lax.cond(fits, by_cp_owner, by_set_owner, values)


PATH = ("x", "zh", "y", "c")


def solution(mesh):
    fine = Mesh(mesh.devices.reshape(4, 2, 4, 2, -1), PATH + ("trade",))
    return jax.shard_map(
        per_device,
        mesh=fine,
        in_specs=(
            P(PATH, None),
            P(PATH, "trade"),
            P(PATH, "trade"),
            P("trade", None),
            P("trade"),
            P("trade"),
            P("trade"),
        ),
        out_specs=P("trade", PATH),
        check_vma=False,
    )
```

```python
import jax
import jax.numpy as jnp
from jax import lax
from jax.sharding import Mesh, PartitionSpec as P

CP_DEV = 32
ROOM = 304


def clenshaw(chosen, coeffs_t):
    x = jnp.tanh(chosen.astype(jnp.float32) * 0.5)
    twice = x + x
    terms = coeffs_t.shape[0]
    b1 = jnp.zeros_like(x)
    b2 = jnp.zeros_like(x)
    for k in range(terms - 1, 0, -1):
        b1, b2 = coeffs_t[k][None, :] + twice * b1 - b2, b1
    return (coeffs_t[0][None, :] + x * b1 - b2).astype(jnp.bfloat16)


def regroup(trade_col, width, owners):
    count = trade_col.shape[0]
    per = count // owners
    block = trade_col // width
    onehot = (block[:, None] == jnp.arange(owners, dtype=jnp.int32)[None, :]).astype(jnp.bfloat16)
    lower = (
        jnp.arange(count, dtype=jnp.int32)[:, None] >= jnp.arange(count, dtype=jnp.int32)[None, :]
    ).astype(jnp.bfloat16)
    running = jnp.dot(lower, onehot, preferred_element_type=jnp.float32)
    rank = jnp.sum(running * onehot.astype(jnp.float32), axis=1).astype(jnp.int32) - 1
    slot = block * per + rank
    return (slot[:, None] == jnp.arange(count, dtype=jnp.int32)[None, :]).astype(jnp.float32)


def ring_reduce(parts, owners):
    ring = list(range(0, owners, 2)) + list(range(owners - 1, 0, -2))
    where = [ring.index(t) for t in range(owners)]
    perm = [(ring[k], ring[(k + 1) % owners]) for k in range(owners)]
    here = jnp.asarray(where, jnp.int32)[lax.axis_index("trade")]
    ring_at = jnp.asarray(ring, jnp.int32)

    def own(step):
        owner = ring_at[(here - 1 - step) % owners]
        return lax.dynamic_index_in_dim(parts, owner, axis=1, keepdims=False)

    acc = own(0)
    for step in range(1, owners):
        acc = lax.ppermute(acc, "trade", perm) + own(step)
    return acc


def per_device(drivers, loadings, start_state, coeffs, trade_col, trade_ns, ns_cp):
    owners = lax.axis_size("trade")
    width = start_state.shape[1]
    count, terms = coeffs.shape
    per = count // owners

    place = regroup(trade_col, width, owners)
    offset = (trade_col % width).astype(jnp.float32)
    table = jnp.concatenate(
        [coeffs.astype(jnp.float32), offset[:, None], trade_ns.astype(jnp.float32)[:, None]], axis=1
    )
    sent = jnp.dot(place.T, table, precision=lax.Precision.HIGHEST)
    sets = ns_cp.shape[0]
    spread = jnp.broadcast_to(ns_cp.astype(jnp.float32).reshape(sets // per, per).T, (owners, per, sets // per))
    sent = jnp.concatenate([sent.reshape(owners, per, terms + 2), spread], axis=2)
    got = lax.all_to_all(sent, "trade", 0, 0, tiled=False)
    all_cp = got[:, :, terms + 2 :].transpose(0, 2, 1).reshape(owners * sets).astype(jnp.int32)
    got = got[:, :, : terms + 2].reshape(count, terms + 2)
    got_coeffs = got[:, :terms].astype(jnp.bfloat16)
    got_col = got[:, terms].astype(jnp.int32)
    got_ns = got[:, terms + 1].astype(jnp.int32)

    gathered = lax.all_gather(loadings, "zh", axis=0, tiled=True)
    gathered = lax.all_gather(gathered, ("x", "y", "c"), axis=0, tiled=True)
    rows = drivers.shape[0]
    lead = loadings.shape[0]
    sizes = [lax.axis_size(name) for name in PATH]
    order = drivers.reshape(rows, *sizes, lead).transpose(0, 1, 3, 4, 2, 5).reshape(rows, -1)
    moved = jnp.dot(order, gathered, preferred_element_type=jnp.float32)
    factors = (start_state.astype(jnp.float32) + moved).astype(jnp.bfloat16)
    pick = (jnp.arange(width, dtype=jnp.int32)[:, None] == got_col[None, :]).astype(jnp.bfloat16)
    chosen = jnp.dot(factors, pick, preferred_element_type=jnp.float32).astype(jnp.bfloat16)
    values = clenshaw(chosen, got_coeffs.astype(jnp.float32).T)

    def by_set_owner(values):
        total_sets = sets * owners
        net_table = (got_ns[:, None] == jnp.arange(total_sets, dtype=jnp.int32)[None, :]).astype(
            jnp.bfloat16
        )
        netting = jnp.dot(values, net_table, preferred_element_type=jnp.float32)
        sent = netting.astype(jnp.bfloat16).reshape(rows, owners, -1)
        shares = jnp.sum(lax.all_to_all(sent, "trade", 1, 1, tiled=False).astype(jnp.float32), axis=1)
        positive = jnp.maximum(shares, 0.0).astype(jnp.bfloat16)
        cp_table = (ns_cp[:, None] == jnp.arange(CP_DEV * owners, dtype=jnp.int32)[None, :]).astype(
            jnp.bfloat16
        )
        partial_cp = jnp.dot(positive, cp_table, preferred_element_type=jnp.float32)
        pieces = lax.all_to_all(partial_cp.reshape(rows, owners, CP_DEV), "trade", 1, 1, tiled=False)
        return jnp.sum(pieces, axis=1).T

    total_sets = sets * owners
    boss = all_cp // CP_DEV
    mask = (boss[:, None] == jnp.arange(owners, dtype=jnp.int32)[None, :]).astype(jnp.bfloat16)
    lower = (
        jnp.arange(total_sets, dtype=jnp.int32)[:, None] >= jnp.arange(total_sets, dtype=jnp.int32)[None, :]
    ).astype(jnp.bfloat16)
    running = jnp.dot(lower, mask, preferred_element_type=jnp.float32)
    rank = jnp.sum(running * mask.astype(jnp.float32), axis=1).astype(jnp.int32) - 1
    fits = jnp.max(rank) < ROOM
    slot = boss * ROOM + rank

    trade_slot = jnp.take(slot, got_ns)
    here = lax.axis_index("trade")
    at_slot = (
        (boss[:, None] == here) & (rank[:, None] == jnp.arange(ROOM, dtype=jnp.int32)[None, :])
    ).astype(jnp.bfloat16)
    of_cp = (all_cp[:, None] == here * CP_DEV + jnp.arange(CP_DEV, dtype=jnp.int32)[None, :]).astype(
        jnp.bfloat16
    )
    cp_table = lax.dot_general(
        of_cp, at_slot, (((0,), (0,)), ((), ())), preferred_element_type=jnp.float32
    ).astype(jnp.bfloat16)

    trade_slot, cp_table = lax.optimization_barrier((trade_slot, cp_table))

    def by_cp_owner(values):
        route = (trade_slot[None, :] == jnp.arange(owners * ROOM, dtype=jnp.int32)[:, None]).astype(
            jnp.bfloat16
        )
        routed = lax.dot_general(
            route, values, (((1,), (1,)), ((), ())), preferred_element_type=jnp.float32
        )
        sent = routed.astype(jnp.bfloat16).reshape(owners, ROOM, rows)
        netting = jnp.sum(lax.all_to_all(sent, "trade", 0, 0, tiled=False).astype(jnp.float32), axis=0)
        positive = jnp.maximum(netting, 0.0).astype(jnp.bfloat16)
        return jnp.dot(cp_table, positive, preferred_element_type=jnp.float32)

    return lax.cond(fits, by_cp_owner, by_set_owner, values)


PATH = ("x", "zh", "y", "c")


def solution(mesh):
    fine = Mesh(mesh.devices.reshape(4, 2, 4, 2, -1), PATH + ("trade",))
    return jax.shard_map(
        per_device,
        mesh=fine,
        in_specs=(
            P(PATH, None),
            P(PATH, "trade"),
            P(PATH, "trade"),
            P("trade", None),
            P("trade"),
            P("trade"),
            P("trade"),
        ),
        out_specs=P("trade", PATH),
        check_vma=False,
    )
```

```python
import jax
import jax.numpy as jnp
from jax import lax
from jax.sharding import Mesh, PartitionSpec as P

CP_DEV = 32
ROOM = 304


def clenshaw(chosen, coeffs_t):
    x = jnp.tanh(chosen.astype(jnp.float32) * 0.5)
    twice = x + x
    terms = coeffs_t.shape[0]
    b1 = jnp.zeros_like(x)
    b2 = jnp.zeros_like(x)
    for k in range(terms - 1, 0, -1):
        b1, b2 = coeffs_t[k][None, :] + twice * b1 - b2, b1
    return (coeffs_t[0][None, :] + x * b1 - b2).astype(jnp.bfloat16)


def regroup(trade_col, width, owners):
    count = trade_col.shape[0]
    per = count // owners
    block = trade_col // width
    onehot = (block[:, None] == jnp.arange(owners, dtype=jnp.int32)[None, :]).astype(jnp.bfloat16)
    lower = (
        jnp.arange(count, dtype=jnp.int32)[:, None] >= jnp.arange(count, dtype=jnp.int32)[None, :]
    ).astype(jnp.bfloat16)
    running = jnp.dot(lower, onehot, preferred_element_type=jnp.float32)
    rank = jnp.sum(running * onehot.astype(jnp.float32), axis=1).astype(jnp.int32) - 1
    slot = block * per + rank
    return (slot[:, None] == jnp.arange(count, dtype=jnp.int32)[None, :]).astype(jnp.float32)


def ring_reduce(parts, owners):
    ring = list(range(0, owners, 2)) + list(range(owners - 1, 0, -2))
    where = [ring.index(t) for t in range(owners)]
    perm = [(ring[k], ring[(k + 1) % owners]) for k in range(owners)]
    here = jnp.asarray(where, jnp.int32)[lax.axis_index("trade")]
    ring_at = jnp.asarray(ring, jnp.int32)

    def own(step):
        owner = ring_at[(here - 1 - step) % owners]
        return lax.dynamic_index_in_dim(parts, owner, axis=1, keepdims=False)

    acc = own(0)
    for step in range(1, owners):
        acc = lax.ppermute(acc, "trade", perm) + own(step)
    return acc


def per_device(drivers, loadings, start_state, coeffs, trade_col, trade_ns, ns_cp):
    owners = lax.axis_size("trade")
    width = start_state.shape[1]
    count, terms = coeffs.shape
    per = count // owners

    place = regroup(trade_col, width, owners)
    offset = (trade_col % width).astype(jnp.float32)
    table = jnp.concatenate(
        [coeffs.astype(jnp.float32), offset[:, None], trade_ns.astype(jnp.float32)[:, None]], axis=1
    )
    sent = jnp.dot(place.T, table, precision=lax.Precision.HIGHEST)
    sets = ns_cp.shape[0]
    spread = jnp.broadcast_to(ns_cp.astype(jnp.float32).reshape(sets // per, per).T, (owners, per, sets // per))
    sent = jnp.concatenate([sent.reshape(owners, per, terms + 2), spread], axis=2)
    got = lax.all_to_all(sent, "trade", 0, 0, tiled=False)
    all_cp = got[:, :, terms + 2 :].transpose(0, 2, 1).reshape(owners * sets).astype(jnp.int32)
    got = got[:, :, : terms + 2].reshape(count, terms + 2)
    got_coeffs = got[:, :terms].astype(jnp.bfloat16)
    got_col = got[:, terms].astype(jnp.int32)
    got_ns = got[:, terms + 1].astype(jnp.int32)

    partner = lax.ppermute(loadings, "zh", [(0, 1), (1, 0)])
    first = lax.axis_index("zh") == 0
    gathered = jnp.where(first, jnp.concatenate([loadings, partner]), jnp.concatenate([partner, loadings]))
    gathered = lax.all_gather(gathered, ("x", "y", "c"), axis=0, tiled=True)
    rows = drivers.shape[0]
    lead = loadings.shape[0]
    sizes = [lax.axis_size(name) for name in PATH]
    order = drivers.reshape(rows, *sizes, lead).transpose(0, 1, 3, 4, 2, 5).reshape(rows, -1)
    moved = jnp.dot(order, gathered, preferred_element_type=jnp.float32)
    factors = (start_state.astype(jnp.float32) + moved).astype(jnp.bfloat16)
    pick = (jnp.arange(width, dtype=jnp.int32)[:, None] == got_col[None, :]).astype(jnp.bfloat16)
    chosen = jnp.dot(factors, pick, preferred_element_type=jnp.float32).astype(jnp.bfloat16)
    values = clenshaw(chosen, got_coeffs.astype(jnp.float32).T)

    def by_set_owner(values):
        total_sets = sets * owners
        net_table = (got_ns[:, None] == jnp.arange(total_sets, dtype=jnp.int32)[None, :]).astype(
            jnp.bfloat16
        )
        netting = jnp.dot(values, net_table, preferred_element_type=jnp.float32)
        sent = netting.astype(jnp.bfloat16).reshape(rows, owners, -1)
        shares = jnp.sum(lax.all_to_all(sent, "trade", 1, 1, tiled=False).astype(jnp.float32), axis=1)
        positive = jnp.maximum(shares, 0.0).astype(jnp.bfloat16)
        cp_table = (ns_cp[:, None] == jnp.arange(CP_DEV * owners, dtype=jnp.int32)[None, :]).astype(
            jnp.bfloat16
        )
        partial_cp = jnp.dot(positive, cp_table, preferred_element_type=jnp.float32)
        pieces = lax.all_to_all(partial_cp.reshape(rows, owners, CP_DEV), "trade", 1, 1, tiled=False)
        return jnp.sum(pieces, axis=1).T

    total_sets = sets * owners
    boss = all_cp // CP_DEV
    mask = (boss[:, None] == jnp.arange(owners, dtype=jnp.int32)[None, :]).astype(jnp.bfloat16)
    lower = (
        jnp.arange(total_sets, dtype=jnp.int32)[:, None] >= jnp.arange(total_sets, dtype=jnp.int32)[None, :]
    ).astype(jnp.bfloat16)
    running = jnp.dot(lower, mask, preferred_element_type=jnp.float32)
    rank = jnp.sum(running * mask.astype(jnp.float32), axis=1).astype(jnp.int32) - 1
    fits = jnp.max(rank) < ROOM
    slot = boss * ROOM + rank

    trade_slot = jnp.take(slot, got_ns)
    here = lax.axis_index("trade")
    at_slot = (
        (boss[:, None] == here) & (rank[:, None] == jnp.arange(ROOM, dtype=jnp.int32)[None, :])
    ).astype(jnp.bfloat16)
    of_cp = (all_cp[:, None] == here * CP_DEV + jnp.arange(CP_DEV, dtype=jnp.int32)[None, :]).astype(
        jnp.bfloat16
    )
    cp_table = lax.dot_general(
        of_cp, at_slot, (((0,), (0,)), ((), ())), preferred_element_type=jnp.float32
    ).astype(jnp.bfloat16)

    trade_slot, cp_table = lax.optimization_barrier((trade_slot, cp_table))

    def by_cp_owner(values):
        route = (trade_slot[None, :] == jnp.arange(owners * ROOM, dtype=jnp.int32)[:, None]).astype(
            jnp.bfloat16
        )
        routed = lax.dot_general(
            route, values, (((1,), (1,)), ((), ())), preferred_element_type=jnp.float32
        )
        sent = routed.astype(jnp.bfloat16).reshape(owners, ROOM, rows)
        netting = jnp.sum(lax.all_to_all(sent, "trade", 0, 0, tiled=False).astype(jnp.float32), axis=0)
        positive = jnp.maximum(netting, 0.0).astype(jnp.bfloat16)
        return jnp.dot(cp_table, positive, preferred_element_type=jnp.float32)

    return lax.cond(fits, by_cp_owner, by_set_owner, values)


PATH = ("x", "zh", "y", "c")


def solution(mesh):
    fine = Mesh(mesh.devices.reshape(4, 2, 4, 2, -1), PATH + ("trade",))
    return jax.shard_map(
        per_device,
        mesh=fine,
        in_specs=(
            P(PATH, None),
            P(PATH, "trade"),
            P(PATH, "trade"),
            P("trade", None),
            P("trade"),
            P("trade"),
            P("trade"),
        ),
        out_specs=P("trade", PATH),
        check_vma=False,
    )
```

```python
import jax
import jax.numpy as jnp
from jax import lax
from jax.sharding import Mesh, PartitionSpec as P

CP_DEV = 32
ROOM = 304


def clenshaw(chosen, coeffs_t):
    x = jnp.tanh(chosen.astype(jnp.float32) * 0.5)
    twice = x + x
    terms = coeffs_t.shape[0]
    b1 = jnp.zeros_like(x)
    b2 = jnp.zeros_like(x)
    for k in range(terms - 1, 0, -1):
        b1, b2 = coeffs_t[k][None, :] + twice * b1 - b2, b1
    return (coeffs_t[0][None, :] + x * b1 - b2).astype(jnp.bfloat16)


def regroup(trade_col, width, owners):
    count = trade_col.shape[0]
    per = count // owners
    block = trade_col // width
    onehot = (block[:, None] == jnp.arange(owners, dtype=jnp.int32)[None, :]).astype(jnp.bfloat16)
    lower = (
        jnp.arange(count, dtype=jnp.int32)[:, None] >= jnp.arange(count, dtype=jnp.int32)[None, :]
    ).astype(jnp.bfloat16)
    running = jnp.dot(lower, onehot, preferred_element_type=jnp.float32)
    rank = jnp.sum(running * onehot.astype(jnp.float32), axis=1).astype(jnp.int32) - 1
    slot = block * per + rank
    return (slot[:, None] == jnp.arange(count, dtype=jnp.int32)[None, :]).astype(jnp.float32)


def ring_reduce(parts, owners):
    ring = list(range(0, owners, 2)) + list(range(owners - 1, 0, -2))
    where = [ring.index(t) for t in range(owners)]
    perm = [(ring[k], ring[(k + 1) % owners]) for k in range(owners)]
    here = jnp.asarray(where, jnp.int32)[lax.axis_index("trade")]
    ring_at = jnp.asarray(ring, jnp.int32)

    def own(step):
        owner = ring_at[(here - 1 - step) % owners]
        return lax.dynamic_index_in_dim(parts, owner, axis=1, keepdims=False)

    acc = own(0)
    for step in range(1, owners):
        acc = lax.ppermute(acc, "trade", perm) + own(step)
    return acc


def per_device(drivers, loadings, start_state, coeffs, trade_col, trade_ns, ns_cp):
    owners = lax.axis_size("trade")
    width = start_state.shape[1]
    count, terms = coeffs.shape
    per = count // owners

    place = regroup(trade_col, width, owners)
    offset = (trade_col % width).astype(jnp.float32)
    table = jnp.concatenate(
        [coeffs.astype(jnp.float32), offset[:, None], trade_ns.astype(jnp.float32)[:, None]], axis=1
    )
    sent = jnp.dot(place.T, table, precision=lax.Precision.HIGHEST)
    sets = ns_cp.shape[0]
    spread = jnp.broadcast_to(ns_cp.astype(jnp.float32).reshape(sets // per, per).T, (owners, per, sets // per))
    sent = jnp.concatenate([sent.reshape(owners, per, terms + 2), spread], axis=2)
    got = lax.all_to_all(sent, "trade", 0, 0, tiled=False)
    all_cp = got[:, :, terms + 2 :].transpose(0, 2, 1).reshape(owners * sets).astype(jnp.int32)
    got = got[:, :, : terms + 2].reshape(count, terms + 2)
    got_coeffs = got[:, :terms].astype(jnp.bfloat16)
    got_col = got[:, terms].astype(jnp.int32)
    got_ns = got[:, terms + 1].astype(jnp.int32)

    gathered = lax.all_gather(loadings, "zh", axis=0, tiled=True)
    gathered = lax.all_gather(gathered, ("x", "y", "c"), axis=0, tiled=True)
    rows = drivers.shape[0]
    lead = loadings.shape[0]
    sizes = [lax.axis_size(name) for name in PATH]
    order = drivers.reshape(rows, *sizes, lead).transpose(0, 1, 3, 4, 2, 5).reshape(rows, -1)
    moved = jnp.dot(order, gathered, preferred_element_type=jnp.float32)
    factors = (start_state.astype(jnp.float32) + moved).astype(jnp.bfloat16)
    pick = (jnp.arange(width, dtype=jnp.int32)[:, None] == got_col[None, :]).astype(jnp.bfloat16)
    chosen = jnp.dot(factors, pick, preferred_element_type=jnp.float32).astype(jnp.bfloat16)
    values = clenshaw(chosen, got_coeffs.astype(jnp.float32).T)

    def by_set_owner(values):
        total_sets = sets * owners
        net_table = (got_ns[:, None] == jnp.arange(total_sets, dtype=jnp.int32)[None, :]).astype(
            jnp.bfloat16
        )
        netting = jnp.dot(values, net_table, preferred_element_type=jnp.float32)
        sent = netting.astype(jnp.bfloat16).reshape(rows, owners, -1)
        shares = jnp.sum(lax.all_to_all(sent, "trade", 1, 1, tiled=False).astype(jnp.float32), axis=1)
        positive = jnp.maximum(shares, 0.0).astype(jnp.bfloat16)
        cp_table = (ns_cp[:, None] == jnp.arange(CP_DEV * owners, dtype=jnp.int32)[None, :]).astype(
            jnp.bfloat16
        )
        partial_cp = jnp.dot(positive, cp_table, preferred_element_type=jnp.float32)
        pieces = lax.all_to_all(partial_cp.reshape(rows, owners, CP_DEV), "trade", 1, 1, tiled=False)
        return jnp.sum(pieces, axis=1).T

    total_sets = sets * owners
    boss = all_cp // CP_DEV
    mask = (boss[:, None] == jnp.arange(owners, dtype=jnp.int32)[None, :]).astype(jnp.bfloat16)
    lower = (
        jnp.arange(total_sets, dtype=jnp.int32)[:, None] >= jnp.arange(total_sets, dtype=jnp.int32)[None, :]
    ).astype(jnp.bfloat16)
    running = jnp.dot(lower, mask, preferred_element_type=jnp.float32)
    rank = jnp.sum(running * mask.astype(jnp.float32), axis=1).astype(jnp.int32) - 1
    fits = jnp.max(rank) < ROOM
    slot = boss * ROOM + rank

    trade_slot = jnp.take(slot, got_ns)
    here = lax.axis_index("trade")
    at_slot = (
        (boss[:, None] == here) & (rank[:, None] == jnp.arange(ROOM, dtype=jnp.int32)[None, :])
    ).astype(jnp.bfloat16)
    of_cp = (all_cp[:, None] == here * CP_DEV + jnp.arange(CP_DEV, dtype=jnp.int32)[None, :]).astype(
        jnp.bfloat16
    )
    cp_table = lax.dot_general(
        of_cp, at_slot, (((0,), (0,)), ((), ())), preferred_element_type=jnp.float32
    ).astype(jnp.bfloat16)

    route = (trade_slot[None, :] == jnp.arange(owners * ROOM, dtype=jnp.int32)[:, None]).astype(jnp.bfloat16)
    route, cp_table = lax.optimization_barrier((route, cp_table))

    def by_cp_owner(values):
        routed = lax.dot_general(
            route, values, (((1,), (1,)), ((), ())), preferred_element_type=jnp.float32
        )
        sent = routed.astype(jnp.bfloat16).reshape(owners, ROOM, rows)
        netting = jnp.sum(lax.all_to_all(sent, "trade", 0, 0, tiled=False).astype(jnp.float32), axis=0)
        positive = jnp.maximum(netting, 0.0).astype(jnp.bfloat16)
        return jnp.dot(cp_table, positive, preferred_element_type=jnp.float32)

    return lax.cond(fits, by_cp_owner, by_set_owner, values)


PATH = ("x", "zh", "y", "c")


def solution(mesh):
    fine = Mesh(mesh.devices.reshape(4, 2, 4, 2, -1), PATH + ("trade",))
    return jax.shard_map(
        per_device,
        mesh=fine,
        in_specs=(
            P(PATH, None),
            P(PATH, "trade"),
            P(PATH, "trade"),
            P("trade", None),
            P("trade"),
            P("trade"),
            P("trade"),
        ),
        out_specs=P("trade", PATH),
        check_vma=False,
    )
```

```python
import jax
import jax.numpy as jnp
from jax import lax
from jax.sharding import Mesh, PartitionSpec as P

CP_DEV = 32
ROOM = 296


def clenshaw(chosen, coeffs_t):
    x = jnp.tanh(chosen.astype(jnp.float32) * 0.5)
    twice = x + x
    terms = coeffs_t.shape[0]
    b1 = jnp.zeros_like(x)
    b2 = jnp.zeros_like(x)
    for k in range(terms - 1, 0, -1):
        b1, b2 = coeffs_t[k][None, :] + twice * b1 - b2, b1
    return (coeffs_t[0][None, :] + x * b1 - b2).astype(jnp.bfloat16)


def regroup(trade_col, width, owners):
    count = trade_col.shape[0]
    per = count // owners
    block = trade_col // width
    onehot = (block[:, None] == jnp.arange(owners, dtype=jnp.int32)[None, :]).astype(jnp.bfloat16)
    lower = (
        jnp.arange(count, dtype=jnp.int32)[:, None] >= jnp.arange(count, dtype=jnp.int32)[None, :]
    ).astype(jnp.bfloat16)
    running = jnp.dot(lower, onehot, preferred_element_type=jnp.float32)
    rank = jnp.sum(running * onehot.astype(jnp.float32), axis=1).astype(jnp.int32) - 1
    slot = block * per + rank
    return (slot[:, None] == jnp.arange(count, dtype=jnp.int32)[None, :]).astype(jnp.float32)


def ring_reduce(parts, owners):
    ring = list(range(0, owners, 2)) + list(range(owners - 1, 0, -2))
    where = [ring.index(t) for t in range(owners)]
    perm = [(ring[k], ring[(k + 1) % owners]) for k in range(owners)]
    here = jnp.asarray(where, jnp.int32)[lax.axis_index("trade")]
    ring_at = jnp.asarray(ring, jnp.int32)

    def own(step):
        owner = ring_at[(here - 1 - step) % owners]
        return lax.dynamic_index_in_dim(parts, owner, axis=1, keepdims=False)

    acc = own(0)
    for step in range(1, owners):
        acc = lax.ppermute(acc, "trade", perm) + own(step)
    return acc


def per_device(drivers, loadings, start_state, coeffs, trade_col, trade_ns, ns_cp):
    owners = lax.axis_size("trade")
    width = start_state.shape[1]
    count, terms = coeffs.shape
    per = count // owners

    place = regroup(trade_col, width, owners)
    offset = (trade_col % width).astype(jnp.float32)
    table = jnp.concatenate(
        [coeffs.astype(jnp.float32), offset[:, None], trade_ns.astype(jnp.float32)[:, None]], axis=1
    )
    sent = jnp.dot(place.T, table, precision=lax.Precision.HIGHEST)
    sets = ns_cp.shape[0]
    spread = jnp.broadcast_to(ns_cp.astype(jnp.float32).reshape(sets // per, per).T, (owners, per, sets // per))
    sent = jnp.concatenate([sent.reshape(owners, per, terms + 2), spread], axis=2)
    got = lax.all_to_all(sent, "trade", 0, 0, tiled=False)
    all_cp = got[:, :, terms + 2 :].transpose(0, 2, 1).reshape(owners * sets).astype(jnp.int32)
    got = got[:, :, : terms + 2].reshape(count, terms + 2)
    got_coeffs = got[:, :terms].astype(jnp.bfloat16)
    got_col = got[:, terms].astype(jnp.int32)
    got_ns = got[:, terms + 1].astype(jnp.int32)

    gathered = lax.all_gather(loadings, "zh", axis=0, tiled=True)
    gathered = lax.all_gather(gathered, ("x", "y", "c"), axis=0, tiled=True)
    rows = drivers.shape[0]
    lead = loadings.shape[0]
    sizes = [lax.axis_size(name) for name in PATH]
    order = drivers.reshape(rows, *sizes, lead).transpose(0, 1, 3, 4, 2, 5).reshape(rows, -1)
    moved = jnp.dot(order, gathered, preferred_element_type=jnp.float32)
    factors = (start_state.astype(jnp.float32) + moved).astype(jnp.bfloat16)
    pick = (jnp.arange(width, dtype=jnp.int32)[:, None] == got_col[None, :]).astype(jnp.bfloat16)
    chosen = jnp.dot(factors, pick, preferred_element_type=jnp.float32).astype(jnp.bfloat16)
    values = clenshaw(chosen, got_coeffs.astype(jnp.float32).T)

    def by_set_owner(values):
        total_sets = sets * owners
        net_table = (got_ns[:, None] == jnp.arange(total_sets, dtype=jnp.int32)[None, :]).astype(
            jnp.bfloat16
        )
        netting = jnp.dot(values, net_table, preferred_element_type=jnp.float32)
        sent = netting.astype(jnp.bfloat16).reshape(rows, owners, -1)
        shares = jnp.sum(lax.all_to_all(sent, "trade", 1, 1, tiled=False).astype(jnp.float32), axis=1)
        positive = jnp.maximum(shares, 0.0).astype(jnp.bfloat16)
        cp_table = (ns_cp[:, None] == jnp.arange(CP_DEV * owners, dtype=jnp.int32)[None, :]).astype(
            jnp.bfloat16
        )
        partial_cp = jnp.dot(positive, cp_table, preferred_element_type=jnp.float32)
        pieces = lax.all_to_all(partial_cp.reshape(rows, owners, CP_DEV), "trade", 1, 1, tiled=False)
        return jnp.sum(pieces, axis=1).T

    total_sets = sets * owners
    boss = all_cp // CP_DEV
    mask = (boss[:, None] == jnp.arange(owners, dtype=jnp.int32)[None, :]).astype(jnp.bfloat16)
    lower = (
        jnp.arange(total_sets, dtype=jnp.int32)[:, None] >= jnp.arange(total_sets, dtype=jnp.int32)[None, :]
    ).astype(jnp.bfloat16)
    running = jnp.dot(lower, mask, preferred_element_type=jnp.float32)
    rank = jnp.sum(running * mask.astype(jnp.float32), axis=1).astype(jnp.int32) - 1
    fits = jnp.max(rank) < ROOM
    slot = boss * ROOM + rank

    trade_slot = jnp.take(slot, got_ns)
    here = lax.axis_index("trade")
    at_slot = (
        (boss[:, None] == here) & (rank[:, None] == jnp.arange(ROOM, dtype=jnp.int32)[None, :])
    ).astype(jnp.bfloat16)
    of_cp = (all_cp[:, None] == here * CP_DEV + jnp.arange(CP_DEV, dtype=jnp.int32)[None, :]).astype(
        jnp.bfloat16
    )
    cp_table = lax.dot_general(
        of_cp, at_slot, (((0,), (0,)), ((), ())), preferred_element_type=jnp.float32
    ).astype(jnp.bfloat16)

    trade_slot, cp_table = lax.optimization_barrier((trade_slot, cp_table))

    def by_cp_owner(values):
        route = (trade_slot[None, :] == jnp.arange(owners * ROOM, dtype=jnp.int32)[:, None]).astype(
            jnp.bfloat16
        )
        routed = lax.dot_general(
            route, values, (((1,), (1,)), ((), ())), preferred_element_type=jnp.float32
        )
        sent = routed.astype(jnp.bfloat16).reshape(owners, ROOM, rows)
        netting = jnp.sum(lax.all_to_all(sent, "trade", 0, 0, tiled=False).astype(jnp.float32), axis=0)
        positive = jnp.maximum(netting, 0.0).astype(jnp.bfloat16)
        return jnp.dot(cp_table, positive, preferred_element_type=jnp.float32)

    return lax.cond(fits, by_cp_owner, by_set_owner, values)


PATH = ("x", "zh", "y", "c")


def solution(mesh):
    fine = Mesh(mesh.devices.reshape(4, 2, 4, 2, -1), PATH + ("trade",))
    return jax.shard_map(
        per_device,
        mesh=fine,
        in_specs=(
            P(PATH, None),
            P(PATH, "trade"),
            P(PATH, "trade"),
            P("trade", None),
            P("trade"),
            P("trade"),
            P("trade"),
        ),
        out_specs=P("trade", PATH),
        check_vma=False,
    )
```
